256 devices in a mesh: cfg: 2 (over z_lo), req: 16 (over y, z_hi), mlp: 8 (over x, core).
Axes of the slice: x: 4, y: 4, z: 8 (z_hi: 4, z_lo: 2; z = z_hi * 2 + z_lo), core: 2. Of those that a mesh axis runs over, the one named last changes fastest.
Arguments:
- hidden: bfloat16 [2, 16384, 1152], P('cfg', ('req', 'mlp')), may hold values from -64 to 64
- noisy_latent: float32 [16384, 16], P(('req', 'mlp'), 'cfg'), may hold values from -6 to 6
- labels: int32 [16, 4], replicated, may hold values from 0 to 999
- timesteps: int32 [16, 4], replicated, may hold values from 0 to 999
- lengths: int32 [16, 4], P('req'), may hold values from 1 to 512, 1024 in all within a row
- guidance: float32 [16, 4], P('req'), may hold values from 1.5 to 4
- keep_scale: float32 [16, 4], P('req'), may hold values from 0.9 to 1.2
- noise_scale: float32 [16, 4], P('req'), may hold values from -0.8 to -0.2
- class_table: bfloat16 [1001, 1152], replicated, may hold values from -6 to 6
- time_up: bfloat16 [256, 1152], replicated, may hold values from -0.375 to 0.375
- time_up_bias: bfloat16 [1152], replicated, may hold values from -4 to 4
- time_out: bfloat16 [1152, 1152], replicated, may hold values from -0.1875 to 0.1875
- time_out_bias: bfloat16 [1152], replicated, may hold values from -4 to 4
- mod_weight: bfloat16 [1152, 9216], P(None, 'req'), may hold values from -0.1875 to 0.1875
- mod_bias: bfloat16 [9216], P('req'), may hold values from -4 to 4
- qkv_weight: bfloat16 [1152, 3456], P(None, 'req'), may hold values from -8 to 8
- qkv_bias: bfloat16 [3456], P('req'), may hold values from -4 to 4
- out_weight: bfloat16 [1152, 1152], P(None, 'req'), may hold values from -0.1875 to 0.1875
- out_bias: bfloat16 [1152], P('req'), may hold values from -4 to 4
- up_weight: bfloat16 [1152, 4608], P(None, 'mlp'), may hold values from -0.1875 to 0.1875
- up_bias: bfloat16 [4608], P('mlp'), may hold values from -4 to 4
- down_weight: bfloat16 [4608, 1152], P('mlp'), may hold values from -1 to 1
- down_bias: bfloat16 [1152], replicated, may hold values from -4 to 4
- final_weight: bfloat16 [1152, 16], replicated, may hold values from -0.1875 to 0.1875
- final_bias: bfloat16 [16], replicated, may hold values from -4 to 4
Outputs:
- next_latent: float32 [16384, 16], P(('req', 'mlp'), 'cfg')
The draws below stay inside these ranges and needn't reach their ends.
Inputs may be any that keep to these rules, and one draw needn't show every extreme that they name: `lengths`: each row sums to 1024, and its largest crop has exactly 512 tokens.
All inputs are finite; a program needn't handle non-finite values.
Results may differ from the reference program's by a relative error of at most 0.015.
Values may be sent and summed in bfloat16 or wider, within the bound.
No kernel may reach another device: no remote copies, remote signals or barrier semaphores. Data moves between devices by JAX's collectives and lax.ppermute only.
A program may use at most 128 MiB of HBM per device.

```python
import math
import jax
import jax.numpy as jnp
import numpy as np
from jax import lax

D = 1152
HEADS = 16
HEAD_DIM = 72
FF = 4608
CLASSES = 1000
FREQ = 256
PATCH_CH = 16
TRAIN_STEPS = 1000
REQS_GROUP = 4
GROUP_TOK = 1024
REQ_MAX = 512
TOKENS = 16384
MODS = 9216
N_REQ = 16
N_MLP = 8


def draw_hidden(key, part):
    keys_list = jax.random.split(key, 1)
    return jax.random.normal(keys_list[0], (2, TOKENS, D), jnp.float32).astype(jnp.bfloat16)


def draw_qkv_weight(key, part):
    keys_list = jax.random.split(key, 1)
    return (jax.random.normal(keys_list[0], (D, 3 * D), jnp.float32) / math.sqrt(D)).astype(jnp.bfloat16)


def draw_down_weight(key, part):
    keys_list = jax.random.split(key, 2)
    column_sign = (2 * jax.random.randint(keys_list[1], (1, D), 0, 2) - 1).astype(jnp.float32)
    base = jnp.clip(jax.random.normal(keys_list[0], (FF, D), jnp.float32), -6.0, 6.0) / math.sqrt(FF)
    offset = 4.5 / FF
    return (base + offset * column_sign).astype(jnp.bfloat16)


def plant(values, rng, least, high):
    index_at = [jax.random.randint(jax.random.fold_in(rng, axis), (), 0, length) for axis, length in enumerate(values.shape)]
    longest = values.shape.index(max(values.shape))
    neighbour = index_at[:longest] + [(index_at[longest] + 1) % values.shape[longest]] + index_at[longest + 1:]
    return values.at[tuple(index_at)].set(least).at[tuple(neighbour)].set(high)


def steps_of(stream_key, shape, cuts, least, top_value):
    def one(axis_at, shards_of):
        draws = jax.random.uniform(jax.random.fold_in(jax.random.fold_in(stream_key, 6), axis_at), (shards_of,), jnp.float32, least / len(cuts), top_value / len(cuts))
        return jnp.repeat(jnp.exp(draws), shape[axis_at] // shards_of).reshape((-1,) + (1,) * (len(shape) - axis_at - 1))

    level = one(*cuts[0])
    for cut in cuts[1:]:
        level = level * one(*cut)
    return level


def length_profile(number_of, total, most, skew):
    loads = [(1 << 20) // math.isqrt(standing ** skew) + 1 for standing in range(2, number_of + 1)]
    rest, holding = total - most - (number_of - 1), [1] * (number_of - 1)
    while rest > 0:
        free = [i for i in range(number_of - 1) if holding[i] < most]
        pool, left = sum([loads[i] for i in free]), rest
        for i in free:
            addition = min(most - holding[i], max(1, left * loads[i] // pool), rest)
            holding[i] = holding[i] + addition
            rest = rest - addition
    return np.array([most] + holding)


def uneven(key, number_of, total, reach, slope):
    if number_of == 2:
        one = jax.random.randint(key, (), max(1, total - reach), min(reach, total - 1) + 1)
        return jnp.stack([one, total - one])
    tallies = jnp.asarray(length_profile(number_of, total, reach, slope), jnp.int32)
    pairs = (number_of - 1) // 2
    donor, sink = tallies[1:1 + 2 * pairs:2], tallies[2:2 + 2 * pairs:2]
    slack = jnp.minimum(donor - 1, reach - sink)
    passed = jax.random.randint(jax.random.fold_in(key, 1), (pairs,), 0, 1 << 20) % (slack + 1)
    tallies = tallies.at[1:1 + 2 * pairs:2].set(donor - passed).at[2:2 + 2 * pairs:2].set(sink + passed)
    return tallies[jax.random.permutation(jax.random.fold_in(key, 2), number_of)]


def centred(rng, dims, scale, most, shards=(), kind=jnp.bfloat16):
    values = jax.random.normal(rng, dims, jnp.float32) * scale
    if len(shards) > 0:
        values = steps_of(rng, dims, shards, -0.22, 0.18) * values
    return jnp.clip(values, min=-most, max=most).astype(kind)


def setup_inputs(seed: int = 0) -> dict:
    key_of = jax.random.split(jax.random.key(seed), 26)
    return {
        "hidden": draw_hidden(jax.random.fold_in(key_of[25], 71), 0),
        "noisy_latent": centred(key_of[1], (TOKENS, PATCH_CH), 1.0, 6.0, ((0, 128), (1, 2)), jnp.float32),
        "labels": plant(jax.random.randint(key_of[2], (N_REQ, REQS_GROUP), 0, CLASSES), jax.random.fold_in(key_of[2], 1), 0, CLASSES - 1).astype(jnp.int32),
        "timesteps": plant(jax.random.randint(key_of[3], (N_REQ, REQS_GROUP), 0, TRAIN_STEPS), jax.random.fold_in(key_of[3], 1), 0, TRAIN_STEPS - 1).astype(jnp.int32),
        "lengths": jax.vmap(lambda own: uneven(own, REQS_GROUP, GROUP_TOK, REQ_MAX, 2))(jax.random.split(key_of[4], N_REQ)).reshape((N_REQ, REQS_GROUP)).astype(jnp.int32),
        "guidance": jnp.clip(1.5 + 2.5 * jax.random.uniform(key_of[5], (N_REQ, REQS_GROUP), jnp.float32) ** steps_of(key_of[5], (N_REQ, REQS_GROUP), ((0, 16),), -0.2, 0.2), 1.5, 4.0),
        "keep_scale": jnp.clip(0.9 + 0.30000007 * jax.random.uniform(key_of[6], (N_REQ, REQS_GROUP), jnp.float32) ** steps_of(key_of[6], (N_REQ, REQS_GROUP), ((0, 16),), -0.2, 0.2), 0.9, 1.2),
        "noise_scale": jnp.clip(-0.8 + 0.6 * jax.random.uniform(key_of[7], (N_REQ, REQS_GROUP), jnp.float32) ** steps_of(key_of[7], (N_REQ, REQS_GROUP), ((0, 16),), -0.2, 0.2), -0.8, -0.2),
        "class_table": centred(key_of[8], (CLASSES + 1, D), 1.0, 6.0),
        "time_up": centred(key_of[9], (FREQ, D), FREQ ** -0.5, 0.375),
        "time_up_bias": centred(key_of[10], (D,), 0.3, 4.0),
        "time_out": centred(key_of[11], (D, D), D ** -0.5, 0.1875),
        "time_out_bias": centred(key_of[12], (D,), 0.3, 4.0),
        "mod_weight": centred(key_of[13], (D, MODS), D ** -0.5, 0.1875, ((1, 16),)),
        "mod_bias": centred(key_of[14], (MODS,), 0.3, 4.0, ((0, 16),)),
        "qkv_weight": draw_qkv_weight(jax.random.fold_in(key_of[25], 71), 0),
        "qkv_bias": centred(key_of[16], (3 * D,), 0.3, 4.0, ((0, 16),)),
        "out_weight": centred(key_of[17], (D, D), D ** -0.5, 0.1875, ((1, 16),)),
        "out_bias": centred(key_of[18], (D,), 0.3, 4.0, ((0, 16),)),
        "up_weight": centred(key_of[19], (D, FF), D ** -0.5, 0.1875, ((1, 8),)),
        "up_bias": centred(key_of[20], (FF,), 0.3, 4.0, ((0, 8),)),
        "down_weight": draw_down_weight(jax.random.fold_in(key_of[25], 71), 0),
        "down_bias": centred(key_of[22], (D,), 0.3, 4.0),
        "final_weight": centred(key_of[23], (D, PATCH_CH), D ** -0.5, 0.1875),
        "final_bias": centred(key_of[24], (PATCH_CH,), 0.3, 4.0),
    }


def layer_norm(values):
    values = values.astype(jnp.float32)
    centre = values - lax.optimization_barrier(jnp.mean(values, axis=-1, keepdims=True))
    variance = lax.optimization_barrier(jnp.mean(centre * centre, axis=-1, keepdims=True))
    return centre * lax.rsqrt(variance + 1e-06)

def time_features(times_flat):
    half_freq = FREQ // 2
    frequency = jnp.exp(-math.log(10000.0) * jnp.arange(half_freq, dtype=jnp.float32) / half_freq)
    angles = times_flat.astype(jnp.float32)[:, None] * frequency[None, :]
    return jnp.concatenate([jnp.cos(angles), jnp.sin(angles)], axis=1).astype(jnp.bfloat16)

def segment_ids(lengths_row, positions):
    ends = jnp.cumsum(lengths_row)
    return lax.optimization_barrier(jnp.sum((positions[:, None] >= ends[None, :]).astype(jnp.int32), axis=1)).astype(jnp.int32)

def attention(queries, keys_all, values_all, query_segment, key_segment):
    scores = jnp.einsum('qhd,khd->hqk', queries.astype(jnp.float32), keys_all.astype(jnp.float32)) / math.sqrt(HEAD_DIM)
    same = (query_segment[:, None] == key_segment[None, :])[None]
    masked = jnp.where(same, scores, -1e+30)
    row_max = lax.optimization_barrier(jnp.max(masked, axis=2, keepdims=True))
    expo = jnp.where(same, jnp.exp(masked - row_max), 0.0)
    denominator = lax.optimization_barrier(jnp.sum(expo, axis=2))
    weights = expo.astype(jnp.bfloat16)
    mixed = jnp.einsum('hqk,khd->qhd', weights.astype(jnp.float32), values_all.astype(jnp.float32))
    result = mixed / jnp.transpose(denominator)[:, :, None]
    return result.astype(jnp.bfloat16).reshape(queries.shape[0], -1)

def reference(hidden, noisy_latent, labels, timesteps, lengths, guidance, keep_scale, noise_scale, class_table, time_up, time_up_bias, time_out, time_out_bias, mod_weight, mod_bias, qkv_weight, qkv_bias, out_weight, out_bias, up_weight, up_bias, down_weight, down_bias, final_weight, final_bias):
    time_feat = time_features(timesteps.reshape(-1))
    time_mid = jax.nn.silu(jnp.dot(time_feat, time_up, preferred_element_type=jnp.float32) + time_up_bias.astype(jnp.float32)).astype(jnp.bfloat16)
    time_cond = jnp.dot(time_mid, time_out, preferred_element_type=jnp.float32) + time_out_bias.astype(jnp.float32)
    classes = jnp.arange(CLASSES + 1, dtype=jnp.int32)
    one_hot = (labels.reshape(-1)[:, None] == classes[None, :]).astype(jnp.bfloat16)
    class_cond = jnp.dot(one_hot, class_table, preferred_element_type=jnp.float32)
    null_cond = class_table[CLASSES].astype(jnp.float32)
    cond_all = jnp.concatenate([time_cond + class_cond, time_cond + null_cond[None, :]], axis=0)
    cond_act = jax.nn.silu(cond_all).astype(jnp.bfloat16)
    modulation = (jnp.dot(cond_act, mod_weight, preferred_element_type=jnp.float32) + mod_bias.astype(jnp.float32)).astype(jnp.bfloat16)
    modulation = modulation.reshape(2, N_REQ, REQS_GROUP, MODS).transpose(1, 0, 2, 3)
    hidden_groups = hidden.reshape(2, N_REQ, GROUP_TOK, D).transpose(1, 0, 2, 3)
    latent_groups = noisy_latent.reshape(N_REQ, GROUP_TOK, PATCH_CH)
    positions = jnp.arange(GROUP_TOK, dtype=jnp.int32)
    block_width = FF // N_MLP

    def run_block(rows, modul_rows, member, segment):
        per_token = jnp.dot(member.astype(jnp.bfloat16), modul_rows, preferred_element_type=jnp.float32)
        pieces = [per_token[:, index * D:(index + 1) * D] for index in range(8)]
        shift_attn, scale_attn, gate_attn, shift_mlp, scale_mlp, gate_mlp, shift_final, scale_final = pieces
        normed = (layer_norm(rows) * (1.0 + scale_attn) + shift_attn).astype(jnp.bfloat16)
        qkv = (jnp.dot(normed, qkv_weight, preferred_element_type=jnp.float32) + qkv_bias.astype(jnp.float32)).astype(jnp.bfloat16)
        queries = qkv[:, :D].reshape(GROUP_TOK, HEADS, HEAD_DIM)
        keys_all = qkv[:, D:2 * D].reshape(GROUP_TOK, HEADS, HEAD_DIM)
        values_all = qkv[:, 2 * D:].reshape(GROUP_TOK, HEADS, HEAD_DIM)
        attended = attention(queries, keys_all, values_all, segment, segment)
        projected = jnp.dot(attended, out_weight, preferred_element_type=jnp.float32) + out_bias.astype(jnp.float32)
        mid_hidden = (rows.astype(jnp.float32) + gate_attn * projected).astype(jnp.bfloat16)
        normed_mlp = (layer_norm(mid_hidden) * (1.0 + scale_mlp) + shift_mlp).astype(jnp.bfloat16)
        inner = jax.nn.gelu(jnp.dot(normed_mlp, up_weight, preferred_element_type=jnp.float32) + up_bias.astype(jnp.float32), approximate=True).astype(jnp.bfloat16)
        mlp_out = jnp.zeros((GROUP_TOK, D), jnp.float32)
        for shard_index in range(N_MLP):
            lower = shard_index * block_width
            partial_value = jnp.dot(inner[:, lower:lower + block_width], down_weight[lower:lower + block_width], preferred_element_type=jnp.float32).astype(jnp.bfloat16)
            partial_value = lax.optimization_barrier(partial_value)
            mlp_out = mlp_out + partial_value.astype(jnp.float32)
        final_hidden = mid_hidden.astype(jnp.float32) + gate_mlp * (mlp_out + down_bias.astype(jnp.float32))
        normed_final = (layer_norm(final_hidden) * (1.0 + scale_final) + shift_final).astype(jnp.bfloat16)
        return jnp.dot(normed_final, final_weight, preferred_element_type=jnp.float32) + final_bias.astype(jnp.float32)

    def one_group(inputs):
        hidden_pair, modul_pair, lengths_row, guide_row, keep_row, noise_row, latent = inputs
        segment = segment_ids(lengths_row, positions)
        member = segment[:, None] == jnp.arange(REQS_GROUP, dtype=jnp.int32)[None, :]
        eps_cond = run_block(hidden_pair[0], modul_pair[0], member, segment)
        eps_free = run_block(hidden_pair[1], modul_pair[1], member, segment)
        member_f = member.astype(jnp.float32)
        guide_tok = lax.optimization_barrier(jnp.sum(member_f * guide_row[None, :], axis=1, keepdims=True))
        keep_tok = lax.optimization_barrier(jnp.sum(member_f * keep_row[None, :], axis=1, keepdims=True))
        noise_tok = lax.optimization_barrier(jnp.sum(member_f * noise_row[None, :], axis=1, keepdims=True))
        return keep_tok * latent + noise_tok * (eps_free + guide_tok * (eps_cond - eps_free))
    result = lax.map(one_group, (hidden_groups, modulation, lengths, guidance, keep_scale, noise_scale, latent_groups))
    return result.reshape(TOKENS, PATCH_CH)
```

```python
import math

import jax
import jax.numpy as jnp
from jax import lax
from jax.sharding import PartitionSpec as P

HEADS = 16
HEAD_DIM = 72
CLASSES = 1000
FREQ = 256


def layer_norm(values):
    values = values.astype(jnp.float32)
    centre = values - jnp.mean(values, axis=-1, keepdims=True)
    variance = jnp.mean(centre * centre, axis=-1, keepdims=True)
    return centre * lax.rsqrt(variance + 1e-06)


def time_features(times_flat):
    half_freq = FREQ // 2
    frequency = jnp.exp(-math.log(10000.0) * jnp.arange(half_freq, dtype=jnp.float32) / half_freq)
    angles = times_flat.astype(jnp.float32)[:, None] * frequency[None, :]
    return jnp.concatenate([jnp.cos(angles), jnp.sin(angles)], axis=1).astype(jnp.bfloat16)


def segment_ids(lengths_row, positions):
    ends = jnp.cumsum(lengths_row)
    return jnp.sum((positions[:, None] >= ends[None, :]).astype(jnp.int32), axis=1)


def attention(queries, keys_all, values_all, query_segment, key_segment):
    scores = jnp.einsum(
        "qhd,khd->hqk", queries, keys_all, preferred_element_type=jnp.float32
    ) / math.sqrt(HEAD_DIM)
    same = (query_segment[:, None] == key_segment[None, :])[None]
    masked = jnp.where(same, scores, -1e30)
    row_max = jnp.max(masked, axis=2, keepdims=True)
    expo = jnp.where(same, jnp.exp(masked - row_max), 0.0)
    denominator = jnp.sum(expo, axis=2)
    weights = expo.astype(jnp.bfloat16)
    mixed = jnp.einsum("hqk,khd->qhd", weights, values_all, preferred_element_type=jnp.float32)
    result = mixed / jnp.transpose(denominator)[:, :, None]
    return result.astype(jnp.bfloat16).reshape(queries.shape[0], -1)


def shards(
    hidden,
    noisy_latent,
    labels,
    timesteps,
    lengths,
    guidance,
    keep_scale,
    noise_scale,
    class_table,
    time_up,
    time_up_bias,
    time_out,
    time_out_bias,
    mod_weight,
    mod_bias,
    qkv_weight,
    qkv_bias,
    out_weight,
    out_bias,
    up_weight,
    up_bias,
    down_weight,
    down_bias,
    final_weight,
    final_bias,
):
    req_count = lax.axis_size("req")
    mlp_count = lax.axis_size("mlp")
    half_index = lax.axis_index("cfg")
    mlp_index = lax.axis_index("mlp")
    tok_rows = hidden.shape[1]
    width = hidden.shape[2]
    group_rows = tok_rows * mlp_count
    per_group = labels.shape[1]
    time_feat = time_features(timesteps.reshape(-1))
    time_mid = jax.nn.silu(
        jnp.dot(time_feat, time_up, preferred_element_type=jnp.float32)
        + time_up_bias.astype(jnp.float32)
    ).astype(jnp.bfloat16)
    time_cond = jnp.dot(
        time_mid, time_out, preferred_element_type=jnp.float32
    ) + time_out_bias.astype(jnp.float32)
    used_labels = jnp.where(half_index == 0, labels.reshape(-1), CLASSES)
    one_hot = (used_labels[:, None] == jnp.arange(CLASSES + 1, dtype=jnp.int32)[None, :]).astype(
        jnp.bfloat16
    )
    cond_act = jax.nn.silu(
        time_cond + jnp.dot(one_hot, class_table, preferred_element_type=jnp.float32)
    ).astype(jnp.bfloat16)
    local_mod = (
        jnp.dot(cond_act, mod_weight, preferred_element_type=jnp.float32)
        + mod_bias.astype(jnp.float32)
    ).astype(jnp.bfloat16)
    local_mod = local_mod.reshape(req_count, per_group, local_mod.shape[1])
    modulation = lax.all_to_all(local_mod, "req", split_axis=0, concat_axis=2, tiled=True)[0]
    positions = jnp.arange(group_rows, dtype=jnp.int32)
    segment_all = segment_ids(lengths[0], positions)
    segment_own = lax.dynamic_slice_in_dim(segment_all, mlp_index * tok_rows, tok_rows)
    member = segment_own[:, None] == jnp.arange(per_group, dtype=jnp.int32)[None, :]
    per_token = jnp.dot(member.astype(jnp.bfloat16), modulation, preferred_element_type=jnp.float32)
    pieces = [per_token[:, index * width : (index + 1) * width] for index in range(8)]
    shift_attn, scale_attn, gate_attn, shift_mlp, scale_mlp, gate_mlp, shift_final, scale_final = (
        pieces
    )
    rows = hidden[0]
    normed = (layer_norm(rows) * (1.0 + scale_attn) + shift_attn).astype(jnp.bfloat16)
    core = mlp_index % 2
    half_rows = width // 2
    pair = [(index, index ^ 1) for index in range(mlp_count)]

    def split_gather(weight, bias):
        mine = lax.dynamic_slice_in_dim(weight, core * half_rows, half_rows, axis=0)
        bias_rows = jnp.zeros((16, weight.shape[1]), weight.dtype).at[0].set(bias)
        gathered = lax.all_gather(
            jnp.concatenate([mine, bias_rows], axis=0), "req", axis=1, tiled=True
        )
        return gathered, lax.ppermute(gathered, "mlp", pair)

    def split_dot(values, mine, other):
        values_mine = lax.dynamic_slice_in_dim(values, core * half_rows, half_rows, axis=1)
        values_other = lax.dynamic_slice_in_dim(values, (1 - core) * half_rows, half_rows, axis=1)
        return (
            jnp.dot(values_mine, mine[:half_rows], preferred_element_type=jnp.float32)
            + jnp.dot(values_other, other[:half_rows], preferred_element_type=jnp.float32)
            + mine[half_rows].astype(jnp.float32)
        )

    qkv_mine, qkv_other = split_gather(qkv_weight, qkv_bias)
    out_mine, out_other = split_gather(out_weight, out_bias)
    qkv = split_dot(normed, qkv_mine, qkv_other).astype(jnp.bfloat16)
    heads_per = HEADS // mlp_count
    head_cols = heads_per * HEAD_DIM
    packed = jnp.transpose(
        qkv.reshape(tok_rows, 3, mlp_count, head_cols), (0, 2, 1, 3)
    ).reshape(tok_rows, mlp_count * 3 * head_cols)
    own_heads = lax.all_to_all(packed, "mlp", split_axis=1, concat_axis=0, tiled=True)
    attended_heads = attention(
        own_heads[:, :head_cols].reshape(group_rows, heads_per, HEAD_DIM),
        own_heads[:, head_cols : 2 * head_cols].reshape(group_rows, heads_per, HEAD_DIM),
        own_heads[:, 2 * head_cols :].reshape(group_rows, heads_per, HEAD_DIM),
        segment_all,
        segment_all,
    )
    attended = lax.all_to_all(attended_heads, "mlp", split_axis=0, concat_axis=1, tiled=True)
    projected = split_dot(attended, out_mine, out_other)
    mid_hidden = (rows.astype(jnp.float32) + gate_attn * projected).astype(jnp.bfloat16)
    normed_mlp = (layer_norm(mid_hidden) * (1.0 + scale_mlp) + shift_mlp).astype(jnp.bfloat16)
    gathered = lax.all_gather(normed_mlp, "mlp", axis=0, tiled=True)
    inner = jax.nn.gelu(
        jnp.dot(gathered, up_weight, preferred_element_type=jnp.float32)
        + up_bias.astype(jnp.float32),
        approximate=True,
    ).astype(jnp.bfloat16)
    mlp_out = lax.psum_scatter(
        jnp.dot(inner, down_weight, preferred_element_type=jnp.float32).astype(jnp.bfloat16),
        "mlp",
        scatter_dimension=0,
        tiled=True,
    ).astype(jnp.float32)
    final_hidden = mid_hidden.astype(jnp.float32) + gate_mlp * (
        mlp_out + down_bias.astype(jnp.float32)
    )
    normed_final = (layer_norm(final_hidden) * (1.0 + scale_final) + shift_final).astype(
        jnp.bfloat16
    )
    predicted = jnp.dot(
        normed_final, final_weight, preferred_element_type=jnp.float32
    ) + final_bias.astype(jnp.float32)
    halves = lax.all_to_all(predicted[None], "cfg", split_axis=2, concat_axis=0, tiled=True)
    eps_cond = halves[0]
    eps_free = halves[1]
    member_f = member.astype(jnp.float32)
    guide_tok = jnp.sum(member_f * guidance, axis=1, keepdims=True)
    keep_tok = jnp.sum(member_f * keep_scale, axis=1, keepdims=True)
    noise_tok = jnp.sum(member_f * noise_scale, axis=1, keepdims=True)
    return keep_tok * noisy_latent + noise_tok * (eps_free + guide_tok * (eps_cond - eps_free))


def solution(mesh):
    return jax.shard_map(
        shards,
        mesh=mesh,
        in_specs=(
            P("cfg", ("req", "mlp"), None),
            P(("req", "mlp"), "cfg"),
            P(),
            P(),
            P("req", None),
            P("req", None),
            P("req", None),
            P("req", None),
            P(),
            P(),
            P(),
            P(),
            P(),
            P(None, "req"),
            P("req"),
            P(None, "req"),
            P("req"),
            P(None, "req"),
            P("req"),
            P(None, "mlp"),
            P("mlp"),
            P("mlp", None),
            P(),
            P(),
            P(),
        ),
        out_specs=P(("req", "mlp"), "cfg"),
        check_vma=False,
    )
```

```python
import math

import jax
import jax.numpy as jnp
from jax import lax
from jax.sharding import PartitionSpec as P

HEADS = 16
HEAD_DIM = 72
CLASSES = 1000
FREQ = 256


def layer_norm(values):
    values = values.astype(jnp.float32)
    centre = values - jnp.mean(values, axis=-1, keepdims=True)
    variance = jnp.mean(centre * centre, axis=-1, keepdims=True)
    return centre * lax.rsqrt(variance + 1e-06)


def time_features(times_flat):
    half_freq = FREQ // 2
    frequency = jnp.exp(-math.log(10000.0) * jnp.arange(half_freq, dtype=jnp.float32) / half_freq)
    angles = times_flat.astype(jnp.float32)[:, None] * frequency[None, :]
    return jnp.concatenate([jnp.cos(angles), jnp.sin(angles)], axis=1).astype(jnp.bfloat16)


def segment_ids(lengths_row, positions):
    ends = jnp.cumsum(lengths_row)
    return jnp.sum((positions[:, None] >= ends[None, :]).astype(jnp.int32), axis=1)


def attention(queries, keys_all, values_all, query_segment, key_segment):
    scores = jnp.einsum(
        "qhd,khd->hqk", queries, keys_all, preferred_element_type=jnp.float32
    ) / math.sqrt(HEAD_DIM)
    same = (query_segment[:, None] == key_segment[None, :])[None]
    masked = jnp.where(same, scores, -1e30)
    row_max = jnp.max(masked, axis=2, keepdims=True)
    expo = jnp.where(same, jnp.exp(masked - row_max), 0.0)
    denominator = jnp.sum(expo, axis=2)
    weights = expo.astype(jnp.bfloat16)
    mixed = jnp.einsum("hqk,khd->qhd", weights, values_all, preferred_element_type=jnp.float32)
    result = mixed / jnp.transpose(denominator)[:, :, None]
    return result.astype(jnp.bfloat16).reshape(queries.shape[0], -1)


def block_body(
    hidden,
    noisy_latent,
    labels,
    timesteps,
    lengths,
    guidance,
    keep_scale,
    noise_scale,
    class_table,
    time_up,
    time_up_bias,
    time_out,
    time_out_bias,
    mod_weight,
    mod_bias,
    qkv_weight,
    qkv_bias,
    out_weight,
    out_bias,
    up_weight,
    up_bias,
    down_weight,
    down_bias,
    final_weight,
    final_bias,
):
    req_count = lax.axis_size("req")
    mlp_count = lax.axis_size("mlp")
    half_index = lax.axis_index("cfg")
    mlp_index = lax.axis_index("mlp")
    tok_rows = hidden.shape[1]
    width = hidden.shape[2]
    group_rows = tok_rows * mlp_count
    per_group = labels.shape[1]
    time_feat = time_features(timesteps.reshape(-1))
    time_mid = jax.nn.silu(
        jnp.dot(time_feat, time_up, preferred_element_type=jnp.float32)
        + time_up_bias.astype(jnp.float32)
    ).astype(jnp.bfloat16)
    time_cond = jnp.dot(
        time_mid, time_out, preferred_element_type=jnp.float32
    ) + time_out_bias.astype(jnp.float32)
    used_labels = jnp.where(half_index == 0, labels.reshape(-1), CLASSES)
    one_hot = (used_labels[:, None] == jnp.arange(CLASSES + 1, dtype=jnp.int32)[None, :]).astype(
        jnp.bfloat16
    )
    cond_act = jax.nn.silu(
        time_cond + jnp.dot(one_hot, class_table, preferred_element_type=jnp.float32)
    ).astype(jnp.bfloat16)
    local_mod = (
        jnp.dot(cond_act, mod_weight, preferred_element_type=jnp.float32)
        + mod_bias.astype(jnp.float32)
    ).astype(jnp.bfloat16)
    local_mod = local_mod.reshape(req_count, per_group, local_mod.shape[1])
    modulation = lax.all_to_all(local_mod, "req", split_axis=0, concat_axis=2, tiled=True)[0]
    positions = jnp.arange(group_rows, dtype=jnp.int32)
    segment_all = segment_ids(lengths[0], positions)
    segment_own = lax.dynamic_slice_in_dim(segment_all, mlp_index * tok_rows, tok_rows)
    member = segment_own[:, None] == jnp.arange(per_group, dtype=jnp.int32)[None, :]
    per_token = jnp.dot(member.astype(jnp.bfloat16), modulation, preferred_element_type=jnp.float32)
    pieces = [per_token[:, index * width : (index + 1) * width] for index in range(8)]
    shift_attn, scale_attn, gate_attn, shift_mlp, scale_mlp, gate_mlp, shift_final, scale_final = (
        pieces
    )
    rows = hidden[0]
    normed = (layer_norm(rows) * (1.0 + scale_attn) + shift_attn).astype(jnp.bfloat16)
    core = mlp_index % 2
    half_rows = width // 2
    pair = [(index, index ^ 1) for index in range(mlp_count)]

    qkv_cols = qkv_weight.shape[1]
    out_cols = out_weight.shape[1]
    block = jnp.concatenate(
        [
            lax.dynamic_slice_in_dim(qkv_weight, core * half_rows, half_rows, axis=0),
            lax.dynamic_slice_in_dim(out_weight, core * half_rows, half_rows, axis=0),
        ],
        axis=1,
    )
    bias_rows = jnp.zeros((16, qkv_cols + out_cols), block.dtype).at[0].set(
        jnp.concatenate([qkv_bias, out_bias])
    )
    both = lax.all_gather(jnp.concatenate([block, bias_rows], axis=0), "req", axis=1, tiled=True)
    both = both.reshape(half_rows + 16, req_count, qkv_cols + out_cols)
    qkv_mine = both[:, :, :qkv_cols].reshape(half_rows + 16, req_count * qkv_cols)
    out_mine = both[:, :, qkv_cols:].reshape(half_rows + 16, req_count * out_cols)
    qkv_other = lax.ppermute(qkv_mine, "mlp", pair)
    out_other = lax.ppermute(out_mine, "mlp", pair)

    def split_dot(values, mine, other):
        values_mine = lax.dynamic_slice_in_dim(values, core * half_rows, half_rows, axis=1)
        values_other = lax.dynamic_slice_in_dim(values, (1 - core) * half_rows, half_rows, axis=1)
        return (
            jnp.dot(values_mine, mine[:half_rows], preferred_element_type=jnp.float32)
            + jnp.dot(values_other, other[:half_rows], preferred_element_type=jnp.float32)
            + mine[half_rows].astype(jnp.float32)
        )

    qkv = split_dot(normed, qkv_mine, qkv_other).astype(jnp.bfloat16)
    heads_per = HEADS // mlp_count
    head_cols = heads_per * HEAD_DIM
    packed = jnp.transpose(
        qkv.reshape(tok_rows, 3, mlp_count, head_cols), (0, 2, 1, 3)
    ).reshape(tok_rows, mlp_count * 3 * head_cols)
    own_heads = lax.all_to_all(packed, "mlp", split_axis=1, concat_axis=0, tiled=True)
    attended_heads = attention(
        own_heads[:, :head_cols].reshape(group_rows, heads_per, HEAD_DIM),
        own_heads[:, head_cols : 2 * head_cols].reshape(group_rows, heads_per, HEAD_DIM),
        own_heads[:, 2 * head_cols :].reshape(group_rows, heads_per, HEAD_DIM),
        segment_all,
        segment_all,
    )
    attended = lax.all_to_all(attended_heads, "mlp", split_axis=0, concat_axis=1, tiled=True)
    projected = split_dot(attended, out_mine, out_other)
    mid_hidden = (rows.astype(jnp.float32) + gate_attn * projected).astype(jnp.bfloat16)
    normed_mlp = (layer_norm(mid_hidden) * (1.0 + scale_mlp) + shift_mlp).astype(jnp.bfloat16)
    gathered = lax.all_gather(normed_mlp, "mlp", axis=0, tiled=True)
    inner = jax.nn.gelu(
        jnp.dot(gathered, up_weight, preferred_element_type=jnp.float32)
        + up_bias.astype(jnp.float32),
        approximate=True,
    ).astype(jnp.bfloat16)
    mlp_out = lax.psum_scatter(
        jnp.dot(inner, down_weight, preferred_element_type=jnp.float32).astype(jnp.bfloat16),
        "mlp",
        scatter_dimension=0,
        tiled=True,
    ).astype(jnp.float32)
    final_hidden = mid_hidden.astype(jnp.float32) + gate_mlp * (
        mlp_out + down_bias.astype(jnp.float32)
    )
    normed_final = (layer_norm(final_hidden) * (1.0 + scale_final) + shift_final).astype(
        jnp.bfloat16
    )
    predicted = jnp.dot(
        normed_final, final_weight, preferred_element_type=jnp.float32
    ) + final_bias.astype(jnp.float32)
    halves = lax.all_to_all(predicted[None], "cfg", split_axis=2, concat_axis=0, tiled=True)
    eps_cond = halves[0]
    eps_free = halves[1]
    member_f = member.astype(jnp.float32)
    guide_tok = jnp.sum(member_f * guidance, axis=1, keepdims=True)
    keep_tok = jnp.sum(member_f * keep_scale, axis=1, keepdims=True)
    noise_tok = jnp.sum(member_f * noise_scale, axis=1, keepdims=True)
    return keep_tok * noisy_latent + noise_tok * (eps_free + guide_tok * (eps_cond - eps_free))


def solution(mesh):
    return jax.shard_map(
        block_body,
        mesh=mesh,
        in_specs=(
            P("cfg", ("req", "mlp"), None),
            P(("req", "mlp"), "cfg"),
            P(),
            P(),
            P("req", None),
            P("req", None),
            P("req", None),
            P("req", None),
            P(),
            P(),
            P(),
            P(),
            P(),
            P(None, "req"),
            P("req"),
            P(None, "req"),
            P("req"),
            P(None, "req"),
            P("req"),
            P(None, "mlp"),
            P("mlp"),
            P("mlp", None),
            P(),
            P(),
            P(),
        ),
        out_specs=P(("req", "mlp"), "cfg"),
        check_vma=False,
    )
```

```python
import math

import jax
import jax.numpy as jnp
from jax import lax
from jax.sharding import PartitionSpec as P

HEADS = 16
HEAD_DIM = 72
CLASSES = 1000
FREQ = 256


def layer_norm(values):
    values = values.astype(jnp.float32)
    centre = values - jnp.mean(values, axis=-1, keepdims=True)
    variance = jnp.mean(centre * centre, axis=-1, keepdims=True)
    return centre * lax.rsqrt(variance + 1e-06)


def time_features(times_flat):
    half_freq = FREQ // 2
    frequency = jnp.exp(-math.log(10000.0) * jnp.arange(half_freq, dtype=jnp.float32) / half_freq)
    angles = times_flat.astype(jnp.float32)[:, None] * frequency[None, :]
    return jnp.concatenate([jnp.cos(angles), jnp.sin(angles)], axis=1).astype(jnp.bfloat16)


def segment_ids(lengths_row, positions):
    ends = jnp.cumsum(lengths_row)
    return jnp.sum((positions[:, None] >= ends[None, :]).astype(jnp.int32), axis=1)


def attention(queries, keys_all, values_all, query_segment, key_segment):
    scores = jnp.einsum(
        "qhd,khd->hqk", queries, keys_all, preferred_element_type=jnp.float32
    ) / math.sqrt(HEAD_DIM)
    same = (query_segment[:, None] == key_segment[None, :])[None]
    masked = jnp.where(same, scores, -1e30)
    row_max = jnp.max(masked, axis=2, keepdims=True)
    expo = jnp.where(same, jnp.exp(masked - row_max), 0.0)
    denominator = jnp.sum(expo, axis=2)
    weights = expo.astype(jnp.bfloat16)
    mixed = jnp.einsum("hqk,khd->qhd", weights, values_all, preferred_element_type=jnp.float32)
    result = mixed / jnp.transpose(denominator)[:, :, None]
    return result.astype(jnp.bfloat16).reshape(queries.shape[0], -1)


def block_body(
    hidden,
    noisy_latent,
    labels,
    timesteps,
    lengths,
    guidance,
    keep_scale,
    noise_scale,
    class_table,
    time_up,
    time_up_bias,
    time_out,
    time_out_bias,
    mod_weight,
    mod_bias,
    qkv_weight,
    qkv_bias,
    out_weight,
    out_bias,
    up_weight,
    up_bias,
    down_weight,
    down_bias,
    final_weight,
    final_bias,
):
    req_count = lax.axis_size("req")
    mlp_count = lax.axis_size("mlp")
    half_index = lax.axis_index("cfg")
    mlp_index = lax.axis_index("mlp")
    tok_rows = hidden.shape[1]
    width = hidden.shape[2]
    group_rows = tok_rows * mlp_count
    per_group = labels.shape[1]
    time_feat = time_features(timesteps.reshape(-1))
    time_mid = jax.nn.silu(
        jnp.dot(time_feat, time_up, preferred_element_type=jnp.float32)
        + time_up_bias.astype(jnp.float32)
    ).astype(jnp.bfloat16)
    time_cond = jnp.dot(
        time_mid, time_out, preferred_element_type=jnp.float32
    ) + time_out_bias.astype(jnp.float32)
    used_labels = jnp.where(half_index == 0, labels.reshape(-1), CLASSES)
    one_hot = (used_labels[:, None] == jnp.arange(CLASSES + 1, dtype=jnp.int32)[None, :]).astype(
        jnp.bfloat16
    )
    cond_act = jax.nn.silu(
        time_cond + jnp.dot(one_hot, class_table, preferred_element_type=jnp.float32)
    ).astype(jnp.bfloat16)
    local_mod = (
        jnp.dot(cond_act, mod_weight, preferred_element_type=jnp.float32)
        + mod_bias.astype(jnp.float32)
    ).astype(jnp.bfloat16)
    local_mod = local_mod.reshape(req_count, per_group, local_mod.shape[1])
    modulation = lax.all_to_all(local_mod, "req", split_axis=0, concat_axis=2, tiled=True)[0]
    positions = jnp.arange(group_rows, dtype=jnp.int32)
    segment_all = segment_ids(lengths[0], positions)
    segment_own = lax.dynamic_slice_in_dim(segment_all, mlp_index * tok_rows, tok_rows)
    member = segment_own[:, None] == jnp.arange(per_group, dtype=jnp.int32)[None, :]
    per_token = jnp.dot(member.astype(jnp.bfloat16), modulation, preferred_element_type=jnp.float32)
    pieces = [per_token[:, index * width : (index + 1) * width] for index in range(8)]
    shift_attn, scale_attn, gate_attn, shift_mlp, scale_mlp, gate_mlp, shift_final, scale_final = (
        pieces
    )
    rows = hidden[0]
    normed = (layer_norm(rows) * (1.0 + scale_attn) + shift_attn).astype(jnp.bfloat16)
    core = mlp_index % 2
    half_rows = width // 2
    pair = [(index, index ^ 1) for index in range(mlp_count)]

    qkv_cols = qkv_weight.shape[1]
    out_cols = out_weight.shape[1]
    block = jnp.concatenate(
        [
            lax.dynamic_slice_in_dim(qkv_weight, core * half_rows, half_rows, axis=0),
            lax.dynamic_slice_in_dim(out_weight, core * half_rows, half_rows, axis=0),
        ],
        axis=1,
    )
    bias_rows = jnp.zeros((16, qkv_cols + out_cols), block.dtype).at[0].set(
        jnp.concatenate([qkv_bias, out_bias])
    )
    both = lax.all_gather(
        jnp.transpose(jnp.concatenate([block, bias_rows], axis=0)), "req", axis=0, tiled=True
    )
    both_other = lax.ppermute(both, "mlp", pair)
    bias_pick = (jnp.arange(16) == 0).astype(jnp.bfloat16)

    def wide_dot(values):
        values_mine = jnp.concatenate(
            [
                lax.dynamic_slice_in_dim(values, core * half_rows, half_rows, axis=1),
                jnp.broadcast_to(bias_pick, (values.shape[0], 16)),
            ],
            axis=1,
        )
        values_other = jnp.concatenate(
            [
                lax.dynamic_slice_in_dim(values, (1 - core) * half_rows, half_rows, axis=1),
                jnp.zeros((values.shape[0], 16), jnp.bfloat16),
            ],
            axis=1,
        )
        contract = (((1,), (1,)), ((), ()))
        wide = lax.dot_general(
            both, values_mine, contract, preferred_element_type=jnp.float32
        ) + lax.dot_general(both_other, values_other, contract, preferred_element_type=jnp.float32)
        return jnp.transpose(wide).reshape(values.shape[0], req_count, qkv_cols + out_cols)

    qkv = wide_dot(normed)[:, :, :qkv_cols].reshape(tok_rows, req_count * qkv_cols)
    qkv = qkv.astype(jnp.bfloat16)
    heads_per = HEADS // mlp_count
    head_cols = heads_per * HEAD_DIM
    packed = jnp.transpose(
        qkv.reshape(tok_rows, 3, mlp_count, head_cols), (0, 2, 1, 3)
    ).reshape(tok_rows, mlp_count * 3 * head_cols)
    own_heads = lax.all_to_all(packed, "mlp", split_axis=1, concat_axis=0, tiled=True)
    attended_heads = attention(
        own_heads[:, :head_cols].reshape(group_rows, heads_per, HEAD_DIM),
        own_heads[:, head_cols : 2 * head_cols].reshape(group_rows, heads_per, HEAD_DIM),
        own_heads[:, 2 * head_cols :].reshape(group_rows, heads_per, HEAD_DIM),
        segment_all,
        segment_all,
    )
    attended = lax.all_to_all(attended_heads, "mlp", split_axis=0, concat_axis=1, tiled=True)
    projected = wide_dot(attended)[:, :, qkv_cols:].reshape(tok_rows, req_count * out_cols)
    mid_hidden = (rows.astype(jnp.float32) + gate_attn * projected).astype(jnp.bfloat16)
    normed_mlp = (layer_norm(mid_hidden) * (1.0 + scale_mlp) + shift_mlp).astype(jnp.bfloat16)
    gathered = lax.all_to_all(
        jnp.broadcast_to(normed_mlp[None], (mlp_count,) + normed_mlp.shape),
        "mlp",
        split_axis=0,
        concat_axis=0,
        tiled=True,
    ).reshape(group_rows, width)
    inner = jax.nn.gelu(
        jnp.dot(gathered, up_weight, preferred_element_type=jnp.float32)
        + up_bias.astype(jnp.float32),
        approximate=True,
    ).astype(jnp.bfloat16)
    partial_out = jnp.dot(inner, down_weight, preferred_element_type=jnp.float32).astype(
        jnp.bfloat16
    )
    mlp_out = jnp.sum(
        lax.all_to_all(
            partial_out.reshape(mlp_count, tok_rows, width),
            "mlp",
            split_axis=0,
            concat_axis=0,
            tiled=True,
        ).astype(jnp.float32),
        axis=0,
    )
    final_hidden = mid_hidden.astype(jnp.float32) + gate_mlp * (
        mlp_out + down_bias.astype(jnp.float32)
    )
    normed_final = (layer_norm(final_hidden) * (1.0 + scale_final) + shift_final).astype(
        jnp.bfloat16
    )
    predicted = jnp.dot(
        normed_final, final_weight, preferred_element_type=jnp.float32
    ) + final_bias.astype(jnp.float32)
    halves = lax.all_to_all(predicted[None], "cfg", split_axis=2, concat_axis=0, tiled=True)
    eps_cond = halves[0]
    eps_free = halves[1]
    member_f = member.astype(jnp.float32)
    guide_tok = jnp.sum(member_f * guidance, axis=1, keepdims=True)
    keep_tok = jnp.sum(member_f * keep_scale, axis=1, keepdims=True)
    noise_tok = jnp.sum(member_f * noise_scale, axis=1, keepdims=True)
    return keep_tok * noisy_latent + noise_tok * (eps_free + guide_tok * (eps_cond - eps_free))


def solution(mesh):
    return jax.shard_map(
        block_body,
        mesh=mesh,
        in_specs=(
            P("cfg", ("req", "mlp"), None),
            P(("req", "mlp"), "cfg"),
            P(),
            P(),
            P("req", None),
            P("req", None),
            P("req", None),
            P("req", None),
            P(),
            P(),
            P(),
            P(),
            P(),
            P(None, "req"),
            P("req"),
            P(None, "req"),
            P("req"),
            P(None, "req"),
            P("req"),
            P(None, "mlp"),
            P("mlp"),
            P("mlp", None),
            P(),
            P(),
            P(),
        ),
        out_specs=P(("req", "mlp"), "cfg"),
        check_vma=False,
    )
```

```python
import math

import jax
import jax.numpy as jnp
from jax import lax
from jax.sharding import PartitionSpec as P

HEADS = 16
HEAD_DIM = 72
CLASSES = 1000
FREQ = 256


def layer_norm(values):
    values = values.astype(jnp.float32)
    centre = values - jnp.mean(values, axis=-1, keepdims=True)
    variance = jnp.mean(centre * centre, axis=-1, keepdims=True)
    return centre * lax.rsqrt(variance + 1e-06)


def time_features(times_flat):
    half_freq = FREQ // 2
    frequency = jnp.exp(-math.log(10000.0) * jnp.arange(half_freq, dtype=jnp.float32) / half_freq)
    angles = times_flat.astype(jnp.float32)[:, None] * frequency[None, :]
    return jnp.concatenate([jnp.cos(angles), jnp.sin(angles)], axis=1).astype(jnp.bfloat16)


def segment_ids(lengths_row, positions):
    ends = jnp.cumsum(lengths_row)
    return jnp.sum((positions[:, None] >= ends[None, :]).astype(jnp.int32), axis=1)


def attention(queries, keys_all, values_all, query_segment, key_segment):
    scores = jnp.einsum(
        "qhd,khd->hqk", queries, keys_all, preferred_element_type=jnp.float32
    ) / math.sqrt(HEAD_DIM)
    same = (query_segment[:, None] == key_segment[None, :])[None]
    masked = jnp.where(same, scores, -1e30)
    row_max = jnp.max(masked, axis=2, keepdims=True)
    expo = jnp.where(same, jnp.exp(masked - row_max), 0.0)
    denominator = jnp.sum(expo, axis=2)
    weights = expo.astype(jnp.bfloat16)
    mixed = jnp.einsum("hqk,khd->qhd", weights, values_all, preferred_element_type=jnp.float32)
    result = mixed / jnp.transpose(denominator)[:, :, None]
    return result.astype(jnp.bfloat16).reshape(queries.shape[0], -1)


def block_body(
    hidden,
    noisy_latent,
    labels,
    timesteps,
    lengths,
    guidance,
    keep_scale,
    noise_scale,
    class_table,
    time_up,
    time_up_bias,
    time_out,
    time_out_bias,
    mod_weight,
    mod_bias,
    qkv_weight,
    qkv_bias,
    out_weight,
    out_bias,
    up_weight,
    up_bias,
    down_weight,
    down_bias,
    final_weight,
    final_bias,
):
    req_count = lax.axis_size("req")
    mlp_count = lax.axis_size("mlp")
    half_index = lax.axis_index("cfg")
    mlp_index = lax.axis_index("mlp")
    tok_rows = hidden.shape[1]
    width = hidden.shape[2]
    group_rows = tok_rows * mlp_count
    per_group = labels.shape[1]
    time_feat = time_features(timesteps.reshape(-1))
    time_mid = jax.nn.silu(
        jnp.dot(time_feat, time_up, preferred_element_type=jnp.float32)
        + time_up_bias.astype(jnp.float32)
    ).astype(jnp.bfloat16)
    time_cond = jnp.dot(
        time_mid, time_out, preferred_element_type=jnp.float32
    ) + time_out_bias.astype(jnp.float32)
    used_labels = jnp.where(half_index == 0, labels.reshape(-1), CLASSES)
    one_hot = (used_labels[:, None] == jnp.arange(CLASSES + 1, dtype=jnp.int32)[None, :]).astype(
        jnp.bfloat16
    )
    cond_act = jax.nn.silu(
        time_cond + jnp.dot(one_hot, class_table, preferred_element_type=jnp.float32)
    ).astype(jnp.bfloat16)
    local_mod = (
        jnp.dot(cond_act, mod_weight, preferred_element_type=jnp.float32)
        + mod_bias.astype(jnp.float32)
    ).astype(jnp.bfloat16)
    local_mod = local_mod.reshape(req_count, per_group, local_mod.shape[1])
    modulation = lax.all_to_all(local_mod, "req", split_axis=0, concat_axis=2, tiled=True)[0]
    positions = jnp.arange(group_rows, dtype=jnp.int32)
    segment_all = segment_ids(lengths[0], positions)
    segment_own = lax.dynamic_slice_in_dim(segment_all, mlp_index * tok_rows, tok_rows)
    member = segment_own[:, None] == jnp.arange(per_group, dtype=jnp.int32)[None, :]
    per_token = jnp.dot(member.astype(jnp.bfloat16), modulation, preferred_element_type=jnp.float32)
    pieces = [per_token[:, index * width : (index + 1) * width] for index in range(8)]
    shift_attn, scale_attn, gate_attn, shift_mlp, scale_mlp, gate_mlp, shift_final, scale_final = (
        pieces
    )
    rows = hidden[0]
    normed = (layer_norm(rows) * (1.0 + scale_attn) + shift_attn).astype(jnp.bfloat16)
    core = mlp_index % 2
    half_rows = width // 2
    pair = [(index, index ^ 1) for index in range(mlp_count)]

    def half_gather(weight, bias):
        mine = lax.dynamic_slice_in_dim(weight, core * half_rows, half_rows, axis=0)
        bias_rows = jnp.zeros((16, weight.shape[1]), weight.dtype).at[0].set(bias)
        gathered = lax.all_gather(
            jnp.concatenate([mine, bias_rows], axis=0), "req", axis=1, tiled=True
        )
        return gathered

    qkv_mine = half_gather(qkv_weight, qkv_bias)
    out_weight, out_bias, modulation = lax.optimization_barrier((out_weight, out_bias, modulation))
    out_mine = half_gather(out_weight, out_bias)
    qkv_other = lax.ppermute(qkv_mine, "mlp", pair)
    out_other = lax.ppermute(out_mine, "mlp", pair)

    def split_dot(values, mine, other):
        values_mine = lax.dynamic_slice_in_dim(values, core * half_rows, half_rows, axis=1)
        values_other = lax.dynamic_slice_in_dim(values, (1 - core) * half_rows, half_rows, axis=1)
        return (
            jnp.dot(values_mine, mine[:half_rows], preferred_element_type=jnp.float32)
            + jnp.dot(values_other, other[:half_rows], preferred_element_type=jnp.float32)
            + mine[half_rows].astype(jnp.float32)
        )

    qkv = split_dot(normed, qkv_mine, qkv_other).astype(jnp.bfloat16)
    heads_per = HEADS // mlp_count
    head_cols = heads_per * HEAD_DIM
    packed = jnp.transpose(
        qkv.reshape(tok_rows, 3, mlp_count, head_cols), (0, 2, 1, 3)
    ).reshape(tok_rows, mlp_count * 3 * head_cols)
    own_heads = lax.all_to_all(packed, "mlp", split_axis=1, concat_axis=0, tiled=True)
    attended_heads = attention(
        own_heads[:, :head_cols].reshape(group_rows, heads_per, HEAD_DIM),
        own_heads[:, head_cols : 2 * head_cols].reshape(group_rows, heads_per, HEAD_DIM),
        own_heads[:, 2 * head_cols :].reshape(group_rows, heads_per, HEAD_DIM),
        segment_all,
        segment_all,
    )
    attended = lax.all_to_all(attended_heads, "mlp", split_axis=0, concat_axis=1, tiled=True)
    projected = split_dot(attended, out_mine, out_other)
    mid_hidden = (rows.astype(jnp.float32) + gate_attn * projected).astype(jnp.bfloat16)
    normed_mlp = (layer_norm(mid_hidden) * (1.0 + scale_mlp) + shift_mlp).astype(jnp.bfloat16)
    gathered = lax.all_gather(normed_mlp, "mlp", axis=0, tiled=True)
    inner = jax.nn.gelu(
        jnp.dot(gathered, up_weight, preferred_element_type=jnp.float32)
        + up_bias.astype(jnp.float32),
        approximate=True,
    ).astype(jnp.bfloat16)
    mlp_out = lax.psum_scatter(
        jnp.dot(inner, down_weight, preferred_element_type=jnp.float32).astype(jnp.bfloat16),
        "mlp",
        scatter_dimension=0,
        tiled=True,
    ).astype(jnp.float32)
    final_hidden = mid_hidden.astype(jnp.float32) + gate_mlp * (
        mlp_out + down_bias.astype(jnp.float32)
    )
    normed_final = (layer_norm(final_hidden) * (1.0 + scale_final) + shift_final).astype(
        jnp.bfloat16
    )
    predicted = jnp.dot(
        normed_final, final_weight, preferred_element_type=jnp.float32
    ) + final_bias.astype(jnp.float32)
    halves = lax.all_to_all(predicted[None], "cfg", split_axis=2, concat_axis=0, tiled=True)
    eps_cond = halves[0]
    eps_free = halves[1]
    member_f = member.astype(jnp.float32)
    guide_tok = jnp.sum(member_f * guidance, axis=1, keepdims=True)
    keep_tok = jnp.sum(member_f * keep_scale, axis=1, keepdims=True)
    noise_tok = jnp.sum(member_f * noise_scale, axis=1, keepdims=True)
    return keep_tok * noisy_latent + noise_tok * (eps_free + guide_tok * (eps_cond - eps_free))


def solution(mesh):
    return jax.shard_map(
        block_body,
        mesh=mesh,
        in_specs=(
            P("cfg", ("req", "mlp"), None),
            P(("req", "mlp"), "cfg"),
            P(),
            P(),
            P("req", None),
            P("req", None),
            P("req", None),
            P("req", None),
            P(),
            P(),
            P(),
            P(),
            P(),
            P(None, "req"),
            P("req"),
            P(None, "req"),
            P("req"),
            P(None, "req"),
            P("req"),
            P(None, "mlp"),
            P("mlp"),
            P("mlp", None),
            P(),
            P(),
            P(),
        ),
        out_specs=P(("req", "mlp"), "cfg"),
        check_vma=False,
    )
```

```python
import math

import jax
import jax.numpy as jnp
from jax import lax
from jax.sharding import PartitionSpec as P

HEADS = 16
HEAD_DIM = 72
CLASSES = 1000
FREQ = 256


def layer_norm(values):
    values = values.astype(jnp.float32)
    centre = values - jnp.mean(values, axis=-1, keepdims=True)
    variance = jnp.mean(centre * centre, axis=-1, keepdims=True)
    return centre * lax.rsqrt(variance + 1e-06)


def time_features(times_flat):
    half_freq = FREQ // 2
    frequency = jnp.exp(-math.log(10000.0) * jnp.arange(half_freq, dtype=jnp.float32) / half_freq)
    angles = times_flat.astype(jnp.float32)[:, None] * frequency[None, :]
    return jnp.concatenate([jnp.cos(angles), jnp.sin(angles)], axis=1).astype(jnp.bfloat16)


def segment_ids(lengths_row, positions):
    ends = jnp.cumsum(lengths_row)
    return jnp.sum((positions[:, None] >= ends[None, :]).astype(jnp.int32), axis=1)


def attention(queries, keys_all, values_all, query_segment, key_segment):
    scores = jnp.einsum(
        "qhd,khd->hqk", queries, keys_all, preferred_element_type=jnp.float32
    ) / math.sqrt(HEAD_DIM)
    same = (query_segment[:, None] == key_segment[None, :])[None]
    masked = jnp.where(same, scores, -1e30)
    row_max = jnp.max(masked, axis=2, keepdims=True)
    expo = jnp.where(same, jnp.exp(masked - row_max), 0.0)
    denominator = jnp.sum(expo, axis=2)
    weights = expo.astype(jnp.bfloat16)
    mixed = jnp.einsum("hqk,khd->qhd", weights, values_all, preferred_element_type=jnp.float32)
    result = mixed / jnp.transpose(denominator)[:, :, None]
    return result.astype(jnp.bfloat16).reshape(queries.shape[0], -1)


def block_body(
    hidden,
    noisy_latent,
    labels,
    timesteps,
    lengths,
    guidance,
    keep_scale,
    noise_scale,
    class_table,
    time_up,
    time_up_bias,
    time_out,
    time_out_bias,
    mod_weight,
    mod_bias,
    qkv_weight,
    qkv_bias,
    out_weight,
    out_bias,
    up_weight,
    up_bias,
    down_weight,
    down_bias,
    final_weight,
    final_bias,
):
    req_count = lax.axis_size("req")
    mlp_count = lax.axis_size("mlp")
    half_index = lax.axis_index("cfg")
    mlp_index = lax.axis_index("mlp")
    tok_rows = hidden.shape[1]
    width = hidden.shape[2]
    group_rows = tok_rows * mlp_count
    per_group = labels.shape[1]
    time_feat = time_features(timesteps.reshape(-1))
    time_mid = jax.nn.silu(
        jnp.dot(time_feat, time_up, preferred_element_type=jnp.float32)
        + time_up_bias.astype(jnp.float32)
    ).astype(jnp.bfloat16)
    time_cond = jnp.dot(
        time_mid, time_out, preferred_element_type=jnp.float32
    ) + time_out_bias.astype(jnp.float32)
    used_labels = jnp.where(half_index == 0, labels.reshape(-1), CLASSES)
    one_hot = (used_labels[:, None] == jnp.arange(CLASSES + 1, dtype=jnp.int32)[None, :]).astype(
        jnp.bfloat16
    )
    cond_act = jax.nn.silu(
        time_cond + jnp.dot(one_hot, class_table, preferred_element_type=jnp.float32)
    ).astype(jnp.bfloat16)
    local_mod = (
        jnp.dot(cond_act, mod_weight, preferred_element_type=jnp.float32)
        + mod_bias.astype(jnp.float32)
    ).astype(jnp.bfloat16)
    local_mod = local_mod.reshape(req_count, per_group, local_mod.shape[1])
    modulation = lax.all_to_all(local_mod, "req", split_axis=0, concat_axis=2, tiled=True)[0]
    positions = jnp.arange(group_rows, dtype=jnp.int32)
    segment_all = segment_ids(lengths[0], positions)
    segment_own = lax.dynamic_slice_in_dim(segment_all, mlp_index * tok_rows, tok_rows)
    member = segment_own[:, None] == jnp.arange(per_group, dtype=jnp.int32)[None, :]
    per_token = jnp.dot(member.astype(jnp.bfloat16), modulation, preferred_element_type=jnp.float32)
    pieces = [per_token[:, index * width : (index + 1) * width] for index in range(8)]
    shift_attn, scale_attn, gate_attn, shift_mlp, scale_mlp, gate_mlp, shift_final, scale_final = (
        pieces
    )
    rows = hidden[0]
    normed = (layer_norm(rows) * (1.0 + scale_attn) + shift_attn).astype(jnp.bfloat16)
    core = mlp_index % 2
    half_rows = width // 2
    pair = [(index, index ^ 1) for index in range(mlp_count)]

    def half_gather(weight, bias):
        mine = lax.dynamic_slice_in_dim(weight, core * half_rows, half_rows, axis=0)
        bias_rows = jnp.zeros((16, weight.shape[1]), weight.dtype).at[0].set(bias)
        gathered = lax.all_gather(
            jnp.concatenate([mine, bias_rows], axis=0), "req", axis=1, tiled=True
        )
        return gathered

    qkv_mine = half_gather(qkv_weight, qkv_bias)
    out_weight, out_bias, modulation = lax.optimization_barrier((out_weight, out_bias, modulation))
    out_mine = half_gather(out_weight, out_bias)
    qkv_other = lax.ppermute(qkv_mine, "mlp", pair)
    out_other = lax.ppermute(out_mine, "mlp", pair)

    def split_dot(values, mine, other):
        values_mine = lax.dynamic_slice_in_dim(values, core * half_rows, half_rows, axis=1)
        values_other = lax.dynamic_slice_in_dim(values, (1 - core) * half_rows, half_rows, axis=1)
        return (
            jnp.dot(values_mine, mine[:half_rows], preferred_element_type=jnp.float32)
            + jnp.dot(values_other, other[:half_rows], preferred_element_type=jnp.float32)
            + mine[half_rows].astype(jnp.float32)
        )

    qkv = split_dot(normed, qkv_mine, qkv_other).astype(jnp.bfloat16)
    heads_per = HEADS // mlp_count
    head_cols = heads_per * HEAD_DIM
    packed = jnp.transpose(
        qkv.reshape(tok_rows, 3, mlp_count, head_cols), (0, 2, 1, 3)
    ).reshape(tok_rows, mlp_count * 3 * head_cols)
    own_heads = lax.all_to_all(packed, "mlp", split_axis=1, concat_axis=0, tiled=True)
    attended_heads = attention(
        own_heads[:, :head_cols].reshape(group_rows, heads_per, HEAD_DIM),
        own_heads[:, head_cols : 2 * head_cols].reshape(group_rows, heads_per, HEAD_DIM),
        own_heads[:, 2 * head_cols :].reshape(group_rows, heads_per, HEAD_DIM),
        segment_all,
        segment_all,
    )
    attended = lax.all_to_all(attended_heads, "mlp", split_axis=0, concat_axis=1, tiled=True)
    projected = split_dot(attended, out_mine, out_other)
    mid_hidden = (rows.astype(jnp.float32) + gate_attn * projected).astype(jnp.bfloat16)
    normed_mlp = (layer_norm(mid_hidden) * (1.0 + scale_mlp) + shift_mlp).astype(jnp.bfloat16)
    gathered = lax.all_gather(normed_mlp, "mlp", axis=0, tiled=True)
    inner = jax.nn.gelu(
        jnp.dot(gathered, up_weight, preferred_element_type=jnp.float32)
        + up_bias.astype(jnp.float32),
        approximate=True,
    ).astype(jnp.bfloat16)
    mlp_out = lax.psum_scatter(
        jnp.dot(inner, down_weight, preferred_element_type=jnp.float32).astype(jnp.bfloat16),
        "mlp",
        scatter_dimension=0,
        tiled=True,
    ).astype(jnp.float32)
    final_hidden = mid_hidden.astype(jnp.float32) + gate_mlp * (
        mlp_out + down_bias.astype(jnp.float32)
    )
    normed_final = (layer_norm(final_hidden) * (1.0 + scale_final) + shift_final).astype(
        jnp.bfloat16
    )
    predicted = jnp.dot(
        normed_final, final_weight, preferred_element_type=jnp.float32
    ) + final_bias.astype(jnp.float32)
    own_cols = noisy_latent.shape[1]
    kept = lax.dynamic_slice_in_dim(predicted, half_index * own_cols, own_cols, axis=1)
    received = lax.ppermute(
        lax.dynamic_slice_in_dim(predicted, (1 - half_index) * own_cols, own_cols, axis=1),
        "cfg",
        [(0, 1), (1, 0)],
    )
    eps_cond = jnp.where(half_index == 0, kept, received)
    eps_free = jnp.where(half_index == 0, received, kept)
    member_f = member.astype(jnp.float32)
    guide_tok = jnp.sum(member_f * guidance, axis=1, keepdims=True)
    keep_tok = jnp.sum(member_f * keep_scale, axis=1, keepdims=True)
    noise_tok = jnp.sum(member_f * noise_scale, axis=1, keepdims=True)
    return keep_tok * noisy_latent + noise_tok * (eps_free + guide_tok * (eps_cond - eps_free))


def solution(mesh):
    return jax.shard_map(
        block_body,
        mesh=mesh,
        in_specs=(
            P("cfg", ("req", "mlp"), None),
            P(("req", "mlp"), "cfg"),
            P(),
            P(),
            P("req", None),
            P("req", None),
            P("req", None),
            P("req", None),
            P(),
            P(),
            P(),
            P(),
            P(),
            P(None, "req"),
            P("req"),
            P(None, "req"),
            P("req"),
            P(None, "req"),
            P("req"),
            P(None, "mlp"),
            P("mlp"),
            P("mlp", None),
            P(),
            P(),
            P(),
        ),
        out_specs=P(("req", "mlp"), "cfg"),
        check_vma=False,
    )
```

```python
import math

import jax
import jax.numpy as jnp
from jax import lax
from jax.sharding import PartitionSpec as P

HEADS = 16
HEAD_DIM = 72
CLASSES = 1000
FREQ = 256


def layer_norm(values):
    values = values.astype(jnp.float32)
    centre = values - jnp.mean(values, axis=-1, keepdims=True)
    variance = jnp.mean(centre * centre, axis=-1, keepdims=True)
    return centre * lax.rsqrt(variance + 1e-06)


def time_features(times_flat):
    half_freq = FREQ // 2
    frequency = jnp.exp(-math.log(10000.0) * jnp.arange(half_freq, dtype=jnp.float32) / half_freq)
    angles = times_flat.astype(jnp.float32)[:, None] * frequency[None, :]
    return jnp.concatenate([jnp.cos(angles), jnp.sin(angles)], axis=1).astype(jnp.bfloat16)


def segment_ids(lengths_row, positions):
    ends = jnp.cumsum(lengths_row)
    return jnp.sum((positions[:, None] >= ends[None, :]).astype(jnp.int32), axis=1)


def attention(queries, keys_all, values_all, query_segment, key_segment):
    scores = jnp.einsum(
        "qhd,khd->hqk", queries, keys_all, preferred_element_type=jnp.float32
    ) / math.sqrt(HEAD_DIM)
    same = (query_segment[:, None] == key_segment[None, :])[None]
    masked = jnp.where(same, scores, -1e30)
    row_max = jnp.max(masked, axis=2, keepdims=True)
    expo = jnp.where(same, jnp.exp(masked - row_max), 0.0)
    denominator = jnp.sum(expo, axis=2)
    weights = expo.astype(jnp.bfloat16)
    mixed = jnp.einsum("hqk,khd->qhd", weights, values_all, preferred_element_type=jnp.float32)
    result = mixed / jnp.transpose(denominator)[:, :, None]
    return result.astype(jnp.bfloat16).reshape(queries.shape[0], -1)


def block_body(
    hidden,
    noisy_latent,
    labels,
    timesteps,
    lengths,
    guidance,
    keep_scale,
    noise_scale,
    class_table,
    time_up,
    time_up_bias,
    time_out,
    time_out_bias,
    mod_weight,
    mod_bias,
    qkv_weight,
    qkv_bias,
    out_weight,
    out_bias,
    up_weight,
    up_bias,
    down_weight,
    down_bias,
    final_weight,
    final_bias,
):
    req_count = lax.axis_size("req")
    mlp_count = lax.axis_size("mlp")
    half_index = lax.axis_index("cfg")
    mlp_index = lax.axis_index("mlp")
    tok_rows = hidden.shape[1]
    width = hidden.shape[2]
    group_rows = tok_rows * mlp_count
    per_group = labels.shape[1]
    time_feat = time_features(timesteps.reshape(-1))
    time_mid = jax.nn.silu(
        jnp.dot(time_feat, time_up, preferred_element_type=jnp.float32)
        + time_up_bias.astype(jnp.float32)
    ).astype(jnp.bfloat16)
    time_cond = jnp.dot(
        time_mid, time_out, preferred_element_type=jnp.float32
    ) + time_out_bias.astype(jnp.float32)
    used_labels = jnp.where(half_index == 0, labels.reshape(-1), CLASSES)
    one_hot = (used_labels[:, None] == jnp.arange(CLASSES + 1, dtype=jnp.int32)[None, :]).astype(
        jnp.bfloat16
    )
    cond_act = jax.nn.silu(
        time_cond + jnp.dot(one_hot, class_table, preferred_element_type=jnp.float32)
    ).astype(jnp.bfloat16)
    local_mod = (
        jnp.dot(cond_act, mod_weight, preferred_element_type=jnp.float32)
        + mod_bias.astype(jnp.float32)
    ).astype(jnp.bfloat16)
    local_mod = local_mod.reshape(req_count, per_group, local_mod.shape[1])
    modulation = lax.all_to_all(local_mod, "req", split_axis=0, concat_axis=2, tiled=True)[0]
    positions = jnp.arange(group_rows, dtype=jnp.int32)
    segment_all = segment_ids(lengths[0], positions)
    segment_own = lax.dynamic_slice_in_dim(segment_all, mlp_index * tok_rows, tok_rows)
    member = segment_own[:, None] == jnp.arange(per_group, dtype=jnp.int32)[None, :]
    per_token = jnp.dot(member.astype(jnp.bfloat16), modulation, preferred_element_type=jnp.float32)
    pieces = [per_token[:, index * width : (index + 1) * width] for index in range(8)]
    shift_attn, scale_attn, gate_attn, shift_mlp, scale_mlp, gate_mlp, shift_final, scale_final = (
        pieces
    )
    rows = hidden[0]
    normed = (layer_norm(rows) * (1.0 + scale_attn) + shift_attn).astype(jnp.bfloat16)
    core = mlp_index % 2
    half_rows = width // 2
    pair = [(index, index ^ 1) for index in range(mlp_count)]

    def half_gather(weight, bias):
        mine = lax.dynamic_slice_in_dim(weight, core * half_rows, half_rows, axis=0)
        bias_rows = jnp.zeros((16, weight.shape[1]), weight.dtype).at[0].set(bias)
        gathered = lax.all_gather(
            jnp.concatenate([mine, bias_rows], axis=0), "req", axis=1, tiled=True
        )
        return gathered

    qkv_mine = half_gather(qkv_weight, qkv_bias)
    out_weight, out_bias, modulation = lax.optimization_barrier((out_weight, out_bias, modulation))
    out_mine = half_gather(out_weight, out_bias)
    qkv_other = lax.ppermute(qkv_mine, "mlp", pair)
    out_other = lax.ppermute(out_mine, "mlp", pair)

    def split_dot(values, mine, other):
        values_mine = lax.dynamic_slice_in_dim(values, core * half_rows, half_rows, axis=1)
        values_other = lax.dynamic_slice_in_dim(values, (1 - core) * half_rows, half_rows, axis=1)
        return (
            jnp.dot(values_mine, mine[:half_rows], preferred_element_type=jnp.float32)
            + jnp.dot(values_other, other[:half_rows], preferred_element_type=jnp.float32)
            + mine[half_rows].astype(jnp.float32)
        )

    qkv = split_dot(normed, qkv_mine, qkv_other).astype(jnp.bfloat16)
    heads_per = HEADS // mlp_count
    head_cols = heads_per * HEAD_DIM
    packed = jnp.transpose(
        qkv.reshape(tok_rows, 3, mlp_count, head_cols), (0, 2, 1, 3)
    ).reshape(tok_rows, mlp_count * 3 * head_cols)
    own_heads = lax.all_to_all(packed, "mlp", split_axis=1, concat_axis=0, tiled=True)
    attended_heads = attention(
        own_heads[:, :head_cols].reshape(group_rows, heads_per, HEAD_DIM),
        own_heads[:, head_cols : 2 * head_cols].reshape(group_rows, heads_per, HEAD_DIM),
        own_heads[:, 2 * head_cols :].reshape(group_rows, heads_per, HEAD_DIM),
        segment_all,
        segment_all,
    )
    attended = lax.all_to_all(attended_heads, "mlp", split_axis=0, concat_axis=1, tiled=True)
    projected = split_dot(attended, out_mine, out_other)
    mid_hidden = (rows.astype(jnp.float32) + gate_attn * projected).astype(jnp.bfloat16)
    normed_mlp = (layer_norm(mid_hidden) * (1.0 + scale_mlp) + shift_mlp).astype(jnp.bfloat16)
    split = width // 2
    gathered_sc = lax.all_gather(normed_mlp[:, :split], "mlp", axis=0, tiled=True)
    gathered_aa = lax.all_to_all(
        jnp.broadcast_to(normed_mlp[None, :, split:], (mlp_count, tok_rows, width - split)),
        "mlp",
        split_axis=0,
        concat_axis=0,
        tiled=True,
    ).reshape(group_rows, width - split)
    inner = jax.nn.gelu(
        jnp.dot(gathered_sc, up_weight[:split], preferred_element_type=jnp.float32)
        + jnp.dot(gathered_aa, up_weight[split:], preferred_element_type=jnp.float32)
        + up_bias.astype(jnp.float32),
        approximate=True,
    ).astype(jnp.bfloat16)
    partial_out = jnp.dot(inner, down_weight, preferred_element_type=jnp.float32).astype(
        jnp.bfloat16
    )
    reduced_sc = lax.psum_scatter(
        partial_out[:, :split], "mlp", scatter_dimension=0, tiled=True
    ).astype(jnp.float32)
    reduced_aa = jnp.sum(
        lax.all_to_all(
            partial_out[:, split:].reshape(mlp_count, tok_rows, width - split),
            "mlp",
            split_axis=0,
            concat_axis=0,
            tiled=True,
        ).astype(jnp.float32),
        axis=0,
    )
    mlp_out = jnp.concatenate([reduced_sc, reduced_aa], axis=1)
    final_hidden = mid_hidden.astype(jnp.float32) + gate_mlp * (
        mlp_out + down_bias.astype(jnp.float32)
    )
    normed_final = (layer_norm(final_hidden) * (1.0 + scale_final) + shift_final).astype(
        jnp.bfloat16
    )
    predicted = jnp.dot(
        normed_final, final_weight, preferred_element_type=jnp.float32
    ) + final_bias.astype(jnp.float32)
    own_cols = noisy_latent.shape[1]
    kept = lax.dynamic_slice_in_dim(predicted, half_index * own_cols, own_cols, axis=1)
    received = lax.ppermute(
        lax.dynamic_slice_in_dim(predicted, (1 - half_index) * own_cols, own_cols, axis=1),
        "cfg",
        [(0, 1), (1, 0)],
    )
    eps_cond = jnp.where(half_index == 0, kept, received)
    eps_free = jnp.where(half_index == 0, received, kept)
    member_f = member.astype(jnp.float32)
    guide_tok = jnp.sum(member_f * guidance, axis=1, keepdims=True)
    keep_tok = jnp.sum(member_f * keep_scale, axis=1, keepdims=True)
    noise_tok = jnp.sum(member_f * noise_scale, axis=1, keepdims=True)
    return keep_tok * noisy_latent + noise_tok * (eps_free + guide_tok * (eps_cond - eps_free))


def solution(mesh):
    return jax.shard_map(
        block_body,
        mesh=mesh,
        in_specs=(
            P("cfg", ("req", "mlp"), None),
            P(("req", "mlp"), "cfg"),
            P(),
            P(),
            P("req", None),
            P("req", None),
            P("req", None),
            P("req", None),
            P(),
            P(),
            P(),
            P(),
            P(),
            P(None, "req"),
            P("req"),
            P(None, "req"),
            P("req"),
            P(None, "req"),
            P("req"),
            P(None, "mlp"),
            P("mlp"),
            P("mlp", None),
            P(),
            P(),
            P(),
        ),
        out_specs=P(("req", "mlp"), "cfg"),
        check_vma=False,
    )
```

```python
import math

import jax
import jax.numpy as jnp
from jax import lax
from jax.sharding import PartitionSpec as P

HEADS = 16
HEAD_DIM = 72
CLASSES = 1000
FREQ = 256


def layer_norm(values):
    values = values.astype(jnp.float32)
    centre = values - jnp.mean(values, axis=-1, keepdims=True)
    variance = jnp.mean(centre * centre, axis=-1, keepdims=True)
    return centre * lax.rsqrt(variance + 1e-06)


def time_features(times_flat):
    half_freq = FREQ // 2
    frequency = jnp.exp(-math.log(10000.0) * jnp.arange(half_freq, dtype=jnp.float32) / half_freq)
    angles = times_flat.astype(jnp.float32)[:, None] * frequency[None, :]
    return jnp.concatenate([jnp.cos(angles), jnp.sin(angles)], axis=1).astype(jnp.bfloat16)


def segment_ids(lengths_row, positions):
    ends = jnp.cumsum(lengths_row)
    return jnp.sum((positions[:, None] >= ends[None, :]).astype(jnp.int32), axis=1)


def attention(queries, keys_all, values_all, query_segment, key_segment):
    scores = jnp.einsum(
        "qhd,khd->hqk", queries, keys_all, preferred_element_type=jnp.float32
    ) / math.sqrt(HEAD_DIM)
    same = (query_segment[:, None] == key_segment[None, :])[None]
    masked = jnp.where(same, scores, -1e30)
    row_max = jnp.max(masked, axis=2, keepdims=True)
    expo = jnp.where(same, jnp.exp(masked - row_max), 0.0)
    denominator = jnp.sum(expo, axis=2)
    weights = expo.astype(jnp.bfloat16)
    mixed = jnp.einsum("hqk,khd->qhd", weights, values_all, preferred_element_type=jnp.float32)
    result = mixed / jnp.transpose(denominator)[:, :, None]
    return result.astype(jnp.bfloat16).reshape(queries.shape[0], -1)


def block_body(
    hidden,
    noisy_latent,
    labels,
    timesteps,
    lengths,
    guidance,
    keep_scale,
    noise_scale,
    class_table,
    time_up,
    time_up_bias,
    time_out,
    time_out_bias,
    mod_weight,
    mod_bias,
    qkv_weight,
    qkv_bias,
    out_weight,
    out_bias,
    up_weight,
    up_bias,
    down_weight,
    down_bias,
    final_weight,
    final_bias,
):
    req_count = lax.axis_size("req")
    mlp_count = lax.axis_size("mlp")
    half_index = lax.axis_index("cfg")
    mlp_index = lax.axis_index("mlp")
    tok_rows = hidden.shape[1]
    width = hidden.shape[2]
    group_rows = tok_rows * mlp_count
    per_group = labels.shape[1]
    time_feat = time_features(timesteps.reshape(-1))
    time_mid = jax.nn.silu(
        jnp.dot(time_feat, time_up, preferred_element_type=jnp.float32)
        + time_up_bias.astype(jnp.float32)
    ).astype(jnp.bfloat16)
    time_cond = jnp.dot(
        time_mid, time_out, preferred_element_type=jnp.float32
    ) + time_out_bias.astype(jnp.float32)
    used_labels = jnp.where(half_index == 0, labels.reshape(-1), CLASSES)
    one_hot = (used_labels[:, None] == jnp.arange(CLASSES + 1, dtype=jnp.int32)[None, :]).astype(
        jnp.bfloat16
    )
    cond_act = jax.nn.silu(
        time_cond + jnp.dot(one_hot, class_table, preferred_element_type=jnp.float32)
    ).astype(jnp.bfloat16)
    local_mod = (
        jnp.dot(cond_act, mod_weight, preferred_element_type=jnp.float32)
        + mod_bias.astype(jnp.float32)
    ).astype(jnp.bfloat16)
    local_mod = local_mod.reshape(req_count, per_group, local_mod.shape[1])
    modulation = lax.all_to_all(local_mod, "req", split_axis=0, concat_axis=2, tiled=True)[0]
    positions = jnp.arange(group_rows, dtype=jnp.int32)
    segment_all = segment_ids(lengths[0], positions)
    segment_own = lax.dynamic_slice_in_dim(segment_all, mlp_index * tok_rows, tok_rows)
    member = segment_own[:, None] == jnp.arange(per_group, dtype=jnp.int32)[None, :]
    per_token = jnp.dot(member.astype(jnp.bfloat16), modulation, preferred_element_type=jnp.float32)
    pieces = [per_token[:, index * width : (index + 1) * width] for index in range(8)]
    shift_attn, scale_attn, gate_attn, shift_mlp, scale_mlp, gate_mlp, shift_final, scale_final = (
        pieces
    )
    rows = hidden[0]
    normed = (layer_norm(rows) * (1.0 + scale_attn) + shift_attn).astype(jnp.bfloat16)
    core = mlp_index % 2
    half_rows = width // 2
    pair = [(index, index ^ 1) for index in range(mlp_count)]

    def half_gather(weight, bias):
        mine = lax.dynamic_slice_in_dim(weight, core * half_rows, half_rows, axis=0)
        bias_rows = jnp.zeros((16, weight.shape[1]), weight.dtype).at[0].set(bias)
        gathered = lax.all_gather(
            jnp.concatenate([mine, bias_rows], axis=0), "req", axis=1, tiled=True
        )
        return gathered

    qkv_mine = half_gather(qkv_weight, qkv_bias)
    out_ext = jnp.concatenate(
        [
            lax.dynamic_slice_in_dim(out_weight, core * half_rows, half_rows, axis=0),
            jnp.zeros((16, out_weight.shape[1]), out_weight.dtype).at[0].set(out_bias),
        ],
        axis=0,
    )
    req_index = lax.axis_index("req")
    pieces = [out_ext] + [
        lax.ppermute(
            out_ext, "req", [(index, (index + shift) % req_count) for index in range(req_count)]
        )
        for shift in range(1, req_count)
    ]
    reverse = jnp.stack(pieces[::-1])
    ordered = lax.dynamic_slice_in_dim(
        jnp.concatenate([reverse, reverse], axis=0), (req_count - 1 - req_index) % req_count, req_count
    )
    out_mine = jnp.transpose(ordered, (1, 0, 2)).reshape(
        half_rows + 16, req_count * out_weight.shape[1]
    )
    qkv_other = lax.ppermute(qkv_mine, "mlp", pair)
    out_other = lax.ppermute(out_mine, "mlp", pair)

    def split_dot(values, mine, other):
        values_mine = lax.dynamic_slice_in_dim(values, core * half_rows, half_rows, axis=1)
        values_other = lax.dynamic_slice_in_dim(values, (1 - core) * half_rows, half_rows, axis=1)
        return (
            jnp.dot(values_mine, mine[:half_rows], preferred_element_type=jnp.float32)
            + jnp.dot(values_other, other[:half_rows], preferred_element_type=jnp.float32)
            + mine[half_rows].astype(jnp.float32)
        )

    qkv = split_dot(normed, qkv_mine, qkv_other).astype(jnp.bfloat16)
    heads_per = HEADS // mlp_count
    head_cols = heads_per * HEAD_DIM
    packed = jnp.transpose(
        qkv.reshape(tok_rows, 3, mlp_count, head_cols), (0, 2, 1, 3)
    ).reshape(tok_rows, mlp_count * 3 * head_cols)
    own_heads = lax.all_to_all(packed, "mlp", split_axis=1, concat_axis=0, tiled=True)
    attended_heads = attention(
        own_heads[:, :head_cols].reshape(group_rows, heads_per, HEAD_DIM),
        own_heads[:, head_cols : 2 * head_cols].reshape(group_rows, heads_per, HEAD_DIM),
        own_heads[:, 2 * head_cols :].reshape(group_rows, heads_per, HEAD_DIM),
        segment_all,
        segment_all,
    )
    attended = lax.all_to_all(attended_heads, "mlp", split_axis=0, concat_axis=1, tiled=True)
    projected = split_dot(attended, out_mine, out_other)
    mid_hidden = (rows.astype(jnp.float32) + gate_attn * projected).astype(jnp.bfloat16)
    normed_mlp = (layer_norm(mid_hidden) * (1.0 + scale_mlp) + shift_mlp).astype(jnp.bfloat16)
    gathered = lax.all_gather(normed_mlp, "mlp", axis=0, tiled=True)
    inner = jax.nn.gelu(
        jnp.dot(gathered, up_weight, preferred_element_type=jnp.float32)
        + up_bias.astype(jnp.float32),
        approximate=True,
    ).astype(jnp.bfloat16)
    mlp_out = lax.psum_scatter(
        jnp.dot(inner, down_weight, preferred_element_type=jnp.float32).astype(jnp.bfloat16),
        "mlp",
        scatter_dimension=0,
        tiled=True,
    ).astype(jnp.float32)
    final_hidden = mid_hidden.astype(jnp.float32) + gate_mlp * (
        mlp_out + down_bias.astype(jnp.float32)
    )
    normed_final = (layer_norm(final_hidden) * (1.0 + scale_final) + shift_final).astype(
        jnp.bfloat16
    )
    predicted = jnp.dot(
        normed_final, final_weight, preferred_element_type=jnp.float32
    ) + final_bias.astype(jnp.float32)
    own_cols = noisy_latent.shape[1]
    kept = lax.dynamic_slice_in_dim(predicted, half_index * own_cols, own_cols, axis=1)
    received = lax.ppermute(
        lax.dynamic_slice_in_dim(predicted, (1 - half_index) * own_cols, own_cols, axis=1),
        "cfg",
        [(0, 1), (1, 0)],
    )
    eps_cond = jnp.where(half_index == 0, kept, received)
    eps_free = jnp.where(half_index == 0, received, kept)
    member_f = member.astype(jnp.float32)
    guide_tok = jnp.sum(member_f * guidance, axis=1, keepdims=True)
    keep_tok = jnp.sum(member_f * keep_scale, axis=1, keepdims=True)
    noise_tok = jnp.sum(member_f * noise_scale, axis=1, keepdims=True)
    return keep_tok * noisy_latent + noise_tok * (eps_free + guide_tok * (eps_cond - eps_free))


def solution(mesh):
    return jax.shard_map(
        block_body,
        mesh=mesh,
        in_specs=(
            P("cfg", ("req", "mlp"), None),
            P(("req", "mlp"), "cfg"),
            P(),
            P(),
            P("req", None),
            P("req", None),
            P("req", None),
            P("req", None),
            P(),
            P(),
            P(),
            P(),
            P(),
            P(None, "req"),
            P("req"),
            P(None, "req"),
            P("req"),
            P(None, "req"),
            P("req"),
            P(None, "mlp"),
            P("mlp"),
            P("mlp", None),
            P(),
            P(),
            P(),
        ),
        out_specs=P(("req", "mlp"), "cfg"),
        check_vma=False,
    )
```

```python
import math

import jax
import jax.numpy as jnp
from jax import lax
from jax.sharding import PartitionSpec as P

HEADS = 16
HEAD_DIM = 72
CLASSES = 1000
FREQ = 256


def layer_norm(values):
    values = values.astype(jnp.float32)
    centre = values - jnp.mean(values, axis=-1, keepdims=True)
    variance = jnp.mean(centre * centre, axis=-1, keepdims=True)
    return centre * lax.rsqrt(variance + 1e-06)


def time_features(times_flat):
    half_freq = FREQ // 2
    frequency = jnp.exp(-math.log(10000.0) * jnp.arange(half_freq, dtype=jnp.float32) / half_freq)
    angles = times_flat.astype(jnp.float32)[:, None] * frequency[None, :]
    return jnp.concatenate([jnp.cos(angles), jnp.sin(angles)], axis=1).astype(jnp.bfloat16)


def segment_ids(lengths_row, positions):
    ends = jnp.cumsum(lengths_row)
    return jnp.sum((positions[:, None] >= ends[None, :]).astype(jnp.int32), axis=1)


def attention(queries, keys_all, values_all, query_segment, key_segment):
    scores = jnp.einsum(
        "qhd,khd->hqk", queries, keys_all, preferred_element_type=jnp.float32
    ) / math.sqrt(HEAD_DIM)
    same = (query_segment[:, None] == key_segment[None, :])[None]
    masked = jnp.where(same, scores, -1e30)
    row_max = jnp.max(masked, axis=2, keepdims=True)
    expo = jnp.where(same, jnp.exp(masked - row_max), 0.0)
    denominator = jnp.sum(expo, axis=2)
    weights = expo.astype(jnp.bfloat16)
    mixed = jnp.einsum("hqk,khd->qhd", weights, values_all, preferred_element_type=jnp.float32)
    result = mixed / jnp.transpose(denominator)[:, :, None]
    return result.astype(jnp.bfloat16).reshape(queries.shape[0], -1)


def block_body(
    hidden,
    noisy_latent,
    labels,
    timesteps,
    lengths,
    guidance,
    keep_scale,
    noise_scale,
    class_table,
    time_up,
    time_up_bias,
    time_out,
    time_out_bias,
    mod_weight,
    mod_bias,
    qkv_weight,
    qkv_bias,
    out_weight,
    out_bias,
    up_weight,
    up_bias,
    down_weight,
    down_bias,
    final_weight,
    final_bias,
):
    req_count = lax.axis_size("req")
    mlp_count = lax.axis_size("mlp")
    half_index = lax.axis_index("cfg")
    mlp_index = lax.axis_index("mlp")
    tok_rows = hidden.shape[1]
    width = hidden.shape[2]
    group_rows = tok_rows * mlp_count
    per_group = labels.shape[1]
    time_feat = time_features(timesteps.reshape(-1))
    time_mid = jax.nn.silu(
        jnp.dot(time_feat, time_up, preferred_element_type=jnp.float32)
        + time_up_bias.astype(jnp.float32)
    ).astype(jnp.bfloat16)
    time_cond = jnp.dot(
        time_mid, time_out, preferred_element_type=jnp.float32
    ) + time_out_bias.astype(jnp.float32)
    used_labels = jnp.where(half_index == 0, labels.reshape(-1), CLASSES)
    one_hot = (used_labels[:, None] == jnp.arange(CLASSES + 1, dtype=jnp.int32)[None, :]).astype(
        jnp.bfloat16
    )
    cond_act = jax.nn.silu(
        time_cond + jnp.dot(one_hot, class_table, preferred_element_type=jnp.float32)
    ).astype(jnp.bfloat16)
    local_mod = (
        jnp.dot(cond_act, mod_weight, preferred_element_type=jnp.float32)
        + mod_bias.astype(jnp.float32)
    ).astype(jnp.bfloat16)
    local_mod = local_mod.reshape(req_count, per_group, local_mod.shape[1])
    modulation = lax.all_to_all(local_mod, "req", split_axis=0, concat_axis=2, tiled=True)[0]
    positions = jnp.arange(group_rows, dtype=jnp.int32)
    segment_all = segment_ids(lengths[0], positions)
    segment_own = lax.dynamic_slice_in_dim(segment_all, mlp_index * tok_rows, tok_rows)
    member = segment_own[:, None] == jnp.arange(per_group, dtype=jnp.int32)[None, :]
    per_token = jnp.dot(member.astype(jnp.bfloat16), modulation, preferred_element_type=jnp.float32)
    pieces = [per_token[:, index * width : (index + 1) * width] for index in range(8)]
    shift_attn, scale_attn, gate_attn, shift_mlp, scale_mlp, gate_mlp, shift_final, scale_final = (
        pieces
    )
    rows = hidden[0]
    normed = (layer_norm(rows) * (1.0 + scale_attn) + shift_attn).astype(jnp.bfloat16)
    core = mlp_index % 2
    half_rows = width // 2
    pair = [(index, index ^ 1) for index in range(mlp_count)]

    def half_gather(weight, bias):
        mine = lax.dynamic_slice_in_dim(weight, core * half_rows, half_rows, axis=0)
        bias_rows = jnp.zeros((16, weight.shape[1]), weight.dtype).at[0].set(bias)
        gathered = lax.all_gather(
            jnp.concatenate([mine, bias_rows], axis=0), "req", axis=1, tiled=True
        )
        return gathered

    qkv_mine = half_gather(qkv_weight, qkv_bias)
    out_weight, out_bias, modulation = lax.optimization_barrier((out_weight, out_bias, modulation))
    out_mine = half_gather(out_weight, out_bias)
    qkv_other = lax.ppermute(qkv_mine, "mlp", pair)
    out_other = lax.ppermute(out_mine, "mlp", pair)

    bias_pick = (jnp.arange(16) == 0).astype(jnp.bfloat16)

    def split_dot(values, mine, other):
        values_mine = jnp.concatenate(
            [
                lax.dynamic_slice_in_dim(values, core * half_rows, half_rows, axis=1),
                jnp.broadcast_to(bias_pick, (values.shape[0], 16)),
            ],
            axis=1,
        )
        values_other = jnp.concatenate(
            [
                lax.dynamic_slice_in_dim(values, (1 - core) * half_rows, half_rows, axis=1),
                jnp.zeros((values.shape[0], 16), values.dtype),
            ],
            axis=1,
        )
        return jnp.dot(values_mine, mine, preferred_element_type=jnp.float32) + jnp.dot(
            values_other, other, preferred_element_type=jnp.float32
        )

    qkv = split_dot(normed, qkv_mine, qkv_other).astype(jnp.bfloat16)
    heads_per = HEADS // mlp_count
    head_cols = heads_per * HEAD_DIM
    packed = jnp.transpose(
        qkv.reshape(tok_rows, 3, mlp_count, head_cols), (0, 2, 1, 3)
    ).reshape(tok_rows, mlp_count * 3 * head_cols)
    own_heads = lax.all_to_all(packed, "mlp", split_axis=1, concat_axis=0, tiled=True)
    attended_heads = attention(
        own_heads[:, :head_cols].reshape(group_rows, heads_per, HEAD_DIM),
        own_heads[:, head_cols : 2 * head_cols].reshape(group_rows, heads_per, HEAD_DIM),
        own_heads[:, 2 * head_cols :].reshape(group_rows, heads_per, HEAD_DIM),
        segment_all,
        segment_all,
    )
    attended = lax.all_to_all(attended_heads, "mlp", split_axis=0, concat_axis=1, tiled=True)
    projected = split_dot(attended, out_mine, out_other)
    mid_hidden = (rows.astype(jnp.float32) + gate_attn * projected).astype(jnp.bfloat16)
    normed_mlp = (layer_norm(mid_hidden) * (1.0 + scale_mlp) + shift_mlp).astype(jnp.bfloat16)
    gathered = lax.all_gather(normed_mlp, "mlp", axis=0, tiled=True)
    inner = jax.nn.gelu(
        jnp.dot(gathered, up_weight, preferred_element_type=jnp.float32)
        + up_bias.astype(jnp.float32),
        approximate=True,
    ).astype(jnp.bfloat16)
    mlp_out = lax.psum_scatter(
        jnp.dot(inner, down_weight, preferred_element_type=jnp.float32).astype(jnp.bfloat16),
        "mlp",
        scatter_dimension=0,
        tiled=True,
    ).astype(jnp.float32)
    final_hidden = mid_hidden.astype(jnp.float32) + gate_mlp * (
        mlp_out + down_bias.astype(jnp.float32)
    )
    normed_final = (layer_norm(final_hidden) * (1.0 + scale_final) + shift_final).astype(
        jnp.bfloat16
    )
    predicted = jnp.dot(
        normed_final, final_weight, preferred_element_type=jnp.float32
    ) + final_bias.astype(jnp.float32)
    own_cols = noisy_latent.shape[1]
    kept = lax.dynamic_slice_in_dim(predicted, half_index * own_cols, own_cols, axis=1)
    received = lax.ppermute(
        lax.dynamic_slice_in_dim(predicted, (1 - half_index) * own_cols, own_cols, axis=1),
        "cfg",
        [(0, 1), (1, 0)],
    )
    eps_cond = jnp.where(half_index == 0, kept, received)
    eps_free = jnp.where(half_index == 0, received, kept)
    member_f = member.astype(jnp.float32)
    guide_tok = jnp.sum(member_f * guidance, axis=1, keepdims=True)
    keep_tok = jnp.sum(member_f * keep_scale, axis=1, keepdims=True)
    noise_tok = jnp.sum(member_f * noise_scale, axis=1, keepdims=True)
    return keep_tok * noisy_latent + noise_tok * (eps_free + guide_tok * (eps_cond - eps_free))


def solution(mesh):
    return jax.shard_map(
        block_body,
        mesh=mesh,
        in_specs=(
            P("cfg", ("req", "mlp"), None),
            P(("req", "mlp"), "cfg"),
            P(),
            P(),
            P("req", None),
            P("req", None),
            P("req", None),
            P("req", None),
            P(),
            P(),
            P(),
            P(),
            P(),
            P(None, "req"),
            P("req"),
            P(None, "req"),
            P("req"),
            P(None, "req"),
            P("req"),
            P(None, "mlp"),
            P("mlp"),
            P("mlp", None),
            P(),
            P(),
            P(),
        ),
        out_specs=P(("req", "mlp"), "cfg"),
        check_vma=False,
    )
```
